256 devices in a mesh: seq: 32 (over x_lo, z, core), chan: 8 (over x_hi, y).
Axes of the slice: x: 4 (x_hi: 2, x_lo: 2; x = x_hi * 2 + x_lo), y: 4, z: 8, core: 2. Of those that a mesh axis runs over, the one named last changes fastest.
Arguments:
- query_in: bfloat16 [16384, 4096], P('seq', 'chan'), may hold values from -6 to 6
- key_in: bfloat16 [16384, 4096], P('seq', 'chan'), may hold values from -6 to 6
- value_in: bfloat16 [16384, 4096], P('seq', 'chan'), may hold values from -6 to 6
- short_weight: float32 [3, 3, 4096], P(None, None, 'chan'), may hold values from -3.5 to 3.5
- long_filter: float32 [256, 16384], P('chan', 'seq'), may hold values from 0 to 0.5
- skip_gain: float32 [4096], P('chan'), may hold values from 0.5 to 1.5
- w_out: bfloat16 [4096, 8192], P('chan', 'seq'), may hold values from -0.1875 to 0.1875
Outputs:
- mixer_out: bfloat16 [16384, 8192], P('seq', 'chan')
The draws below stay inside these ranges and needn't reach their ends.
All inputs are finite; a program needn't handle non-finite values.
Results may differ from the reference program's by a relative error of at most 0.018.
Values may be sent and summed in bfloat16 or wider, within the bound.
No kernel may reach another device: no remote copies, remote signals or barrier semaphores. Data moves between devices by JAX's collectives and lax.ppermute only.
A program may use at most 128 MiB of HBM per device.

```python
import jax
import jax.numpy as jnp
from jax import lax

D = 8192
DW = 4096
GROUP = 16
KW = 3
LENGTH = 16384
GROUPS = 256
N_CHAN = 8


def draw_long_filter(key, part):
    keys = jax.random.split(key, 6)
    lag_int = jnp.arange(LENGTH, dtype=jnp.int32)
    lag_pos = lag_int.astype(jnp.float32)
    slow_reach = jnp.exp(jax.random.uniform(keys[0], (GROUPS,), jnp.float32, jnp.log(LENGTH * 0.5), jnp.log(LENGTH * 8.0)))
    fast_reach = jax.random.uniform(keys[1], (GROUPS,), jnp.float32, 30.0, 50.0)
    fast = jax.random.randint(keys[2], (GROUPS,), 0, 2) == 0
    rough = jax.random.uniform(keys[3], (GROUPS, LENGTH), jnp.float32, 0.5, 1.5)
    reach = jnp.where(fast, fast_reach, slow_reach)
    spots = jax.random.randint(keys[4], (GROUPS, 3), 0, LENGTH)
    drops = jnp.log(jax.random.uniform(keys[5], (GROUPS, 3), jnp.float32, 0.5, 0.8))
    fallen = jnp.sum(jnp.where(lag_int[None, None, :] >= spots[:, :, None], drops[:, :, None], 0.0), axis=1)
    height = jnp.sqrt(2.0 / jnp.minimum(reach, LENGTH * 1.0))
    return height[:, None] * jnp.exp(-lag_pos[None, :] / reach[:, None] + fallen) * rough


def spiked(drawn, stream_key, source, target, shards_of, factor):
    owner, partner = [(jnp.arange(drawn.shape[axis_at]) // (drawn.shape[axis_at] // shards_of)).reshape([-1 if axis == axis_at else 1 for axis in range(drawn.ndim)]) for axis_at in (source, target)]
    chosen = jax.random.permutation(stream_key, shards_of)[partner]
    strong = (owner == chosen) | (owner == (partner + shards_of // 2) % shards_of)
    return jnp.where(strong, factor * drawn, drawn)


def shard_levels(own_key, dims, shards, smallest, high):
    level = 1.0
    for dim, parts in shards:
        steps = jax.random.uniform(jax.random.fold_in(jax.random.fold_in(own_key, 6), dim), (parts,), jnp.float32, smallest / len(shards), high / len(shards))
        level = level * jnp.repeat(jnp.exp(steps), dims[dim] // parts).reshape((-1,) + (1,) * (len(dims) - 1 - dim))
    return level


def centred(rng, dims, spread, bound, shards=(), kind=jnp.bfloat16):
    values = spread * jax.random.normal(rng, dims, jnp.float32)
    if shards:
        values = values * shard_levels(rng, dims, shards, -0.22, 0.18)
    return jnp.clip(values, -bound, bound).astype(kind)


def bell_draw_with(own_key, dims, spread, most, cuts, heavy, held_as=jnp.bfloat16):
    entries = spread * jax.random.normal(own_key, dims, jnp.float32)
    if cuts:
        entries = entries * shard_levels(own_key, dims, cuts, -0.22, 0.18)
    return jnp.clip(spiked(entries, jax.random.fold_in(own_key, 3), *heavy), -most, most).astype(held_as)


def setup_inputs(seed: int = 0) -> dict:
    splits = jax.random.split(jax.random.key(seed), 8)
    query_in = centred(splits[0], (LENGTH, DW), 1.0, 6.0, ((0, 32), (1, 8)))
    key_in = centred(splits[1], (LENGTH, DW), 1.0, 6.0, ((0, 32), (1, 8)))
    value_in = centred(splits[2], (LENGTH, DW), 1.0, 6.0, ((0, 32), (1, 8)))
    short_weight = centred(splits[3], (3, KW, DW), KW ** -0.5, 3.5, ((2, 8),), jnp.float32)
    long_filter = draw_long_filter(jax.random.fold_in(splits[7], 71), 0)
    skip_gain = jnp.clip(0.5 + 1.0 * jax.random.uniform(splits[5], (DW,), jnp.float32) ** shard_levels(splits[5], (DW,), ((0, 8),), -0.2, 0.2), 0.5, 1.5)
    w_out = bell_draw_with(splits[6], (DW, D), DW ** -0.5, 0.1875, ((0, 8), (1, 32)), (0, 1, 32, 2.75))
    return dict(query_in=query_in, key_in=key_in, value_in=value_in, short_weight=short_weight, long_filter=long_filter, skip_gain=skip_gain, w_out=w_out)


def short_conv(signal, taps):
    padded = jnp.pad(signal.astype(jnp.float32), ((KW - 1, 0), (0, 0)))
    summed = taps[0] * padded[KW - 1: KW - 1 + LENGTH]
    for shift in range(1, KW):
        summed = summed + taps[shift] * padded[KW - 1 - shift: KW - 1 - shift + LENGTH]
    return summed


def group_conv(operands):
    block, filt_row = operands
    spectrum = jnp.fft.rfft(block.astype(jnp.float32), n=2 * LENGTH, axis=0)
    kernel = jnp.fft.rfft(filt_row, n=2 * LENGTH)
    result = jnp.fft.irfft(spectrum * kernel[:, None], n=2 * LENGTH, axis=0)[:LENGTH]
    return result.astype(jnp.bfloat16)


def reference(query_in, key_in, value_in, short_weight, long_filter, skip_gain, w_out):
    query_conv = short_conv(query_in, short_weight[0]).astype(jnp.bfloat16)
    key_conv = short_conv(key_in, short_weight[1])
    value_conv = short_conv(value_in, short_weight[2])
    gated = (key_conv * value_conv).astype(jnp.bfloat16)
    grouped = gated.reshape(LENGTH, GROUPS, GROUP).transpose(1, 0, 2)
    convs = lax.map(group_conv, (grouped, long_filter))
    conv = convs.transpose(1, 0, 2).reshape(LENGTH, DW)
    mixed = (query_conv.astype(jnp.float32) * (conv.astype(jnp.float32) + skip_gain * gated.astype(jnp.float32))).astype(jnp.bfloat16)
    slab = DW // N_CHAN
    summed = jnp.zeros((LENGTH, D), jnp.float32)
    for member in range(N_CHAN):
        first = member * slab
        partial_value = jnp.dot(mixed[:, first:first + slab], w_out[first:first + slab], preferred_element_type=jnp.float32)
        summed = summed + lax.optimization_barrier(partial_value.astype(jnp.bfloat16)).astype(jnp.float32)
    return summed.astype(jnp.bfloat16)
```

```python
import jax
import jax.numpy as jnp
from jax import lax
from jax.sharding import PartitionSpec as P

GROUP = 16
KW = 3


def passed_along(value, axis, by):
    devices = lax.axis_size(axis)
    pairs = [(i, i + by) for i in range(devices) if 0 <= i + by < devices]
    return lax.ppermute(value, axis, pairs)


def toeplitz_blocks(h, parts, block):
    flipped = jnp.concatenate([h[::-1], jnp.zeros((block,), h.dtype)])
    pieces = flipped.reshape(parts + 1, block)[::-1]
    windows = jnp.concatenate([pieces[1:], pieces[:-1]], axis=1)[:, : 2 * block - 1]
    rows = windows.astype(jnp.bfloat16)[None]
    step = 1
    while rows.shape[0] < block:
        width = rows.shape[2] - step
        rows = jnp.concatenate([rows[:, :, step : step + width], rows[:, :, :width]], axis=0)
        step *= 2
    return rows.reshape(block, parts * block)


def long_conv(gated, long_filter):
    block, width = gated.shape
    parts = lax.axis_size("seq")
    sent = gated.T.reshape(parts, width // parts, block)
    signal = lax.all_to_all(sent, "seq", 0, 0, tiled=True)
    taps = lax.all_to_all(long_filter, "seq", 0, 1, tiled=True)
    chans = signal.shape[1]
    filt = toeplitz_blocks(taps[0], parts, block)
    rows = jnp.transpose(signal, (2, 0, 1)).reshape(block, parts * chans)
    padded = jnp.concatenate([jnp.zeros((block, (parts - 1) * chans), rows.dtype), rows], axis=1)
    shifted = jnp.stack(
        [padded[:, (parts - 1 - k) * chans : (2 * parts - 1 - k) * chans] for k in range(parts)]
    )
    shifted = shifted.reshape(parts * block, parts * chans)
    result = jnp.dot(filt, shifted, preferred_element_type=jnp.float32)
    result = result.astype(jnp.bfloat16).T.reshape(parts, chans, block)
    back = lax.all_to_all(result, "seq", 0, 0, tiled=True)
    return back.reshape(parts * chans, block).T


def on_device(query_in, key_in, value_in, short_weight, long_filter, skip_gain, w_out):
    local_len, width = query_in.shape
    stacked = jnp.stack([query_in, key_in, value_in])
    border = passed_along(stacked[:, local_len - (KW - 1) :, :], "seq", 1)
    extended = jnp.concatenate([border, stacked], axis=1)
    convolved = short_weight[:, 0, None, :] * extended[:, KW - 1 : KW - 1 + local_len, :].astype(
        jnp.float32
    )
    for shift in range(1, KW):
        convolved = convolved + short_weight[:, shift, None, :] * extended[
            :, KW - 1 - shift : KW - 1 - shift + local_len, :
        ].astype(jnp.float32)
    query_conv = convolved[0].astype(jnp.bfloat16)
    gated = (convolved[1] * convolved[2]).astype(jnp.bfloat16)
    conv = long_conv(gated, long_filter)
    mixed = (
        query_conv.astype(jnp.float32)
        * (conv.astype(jnp.float32) + skip_gain * gated.astype(jnp.float32))
    ).astype(jnp.bfloat16)
    terms = jnp.dot(
        mixed, lax.all_gather(w_out, "seq", axis=1, tiled=True), preferred_element_type=jnp.float32
    )
    return lax.psum_scatter(terms.astype(jnp.bfloat16), "chan", scatter_dimension=1, tiled=True)


def solution(mesh):
    placed = (
        P("seq", "chan"),
        P("seq", "chan"),
        P("seq", "chan"),
        P(None, None, "chan"),
        P("chan", "seq"),
        P("chan"),
        P("chan", "seq"),
    )
    return jax.shard_map(
        on_device, mesh=mesh, in_specs=placed, out_specs=P("seq", "chan"), check_vma=False
    )
```

```python
import jax
import jax.numpy as jnp
from jax import lax
from jax.sharding import Mesh, PartitionSpec as P

GROUP = 16
KW = 3


def passed_along(value, axis, by):
    devices = lax.axis_size(axis)
    pairs = [(i, i + by) for i in range(devices) if 0 <= i + by < devices]
    return lax.ppermute(value, axis, pairs)


def toeplitz_blocks(h, parts, block):
    flipped = jnp.concatenate([h[::-1], jnp.zeros((block,), h.dtype)])
    pieces = flipped.reshape(parts + 1, block)[::-1]
    windows = jnp.concatenate([pieces[1:], pieces[:-1]], axis=1)[:, : 2 * block - 1]
    rows = windows.astype(jnp.bfloat16)[None]
    step = 1
    while rows.shape[0] < block:
        width = rows.shape[2] - step
        rows = jnp.concatenate([rows[:, :, step : step + width], rows[:, :, :width]], axis=0)
        step *= 2
    return rows.reshape(block, parts * block)


def long_conv(gated, long_filter):
    block, width = gated.shape
    parts = lax.axis_size("seq")
    sent = gated.T.reshape(parts, width // parts, block)
    signal = lax.all_to_all(sent, "seq", 0, 0, tiled=True)
    taps = lax.all_to_all(long_filter, "seq", 0, 1, tiled=True)
    chans = signal.shape[1]
    filt = toeplitz_blocks(taps[0], parts, block)
    rows = jnp.transpose(signal, (2, 0, 1)).reshape(block, parts * chans)
    padded = jnp.concatenate([jnp.zeros((block, (parts - 1) * chans), rows.dtype), rows], axis=1)
    shifted = jnp.stack(
        [padded[:, (parts - 1 - k) * chans : (2 * parts - 1 - k) * chans] for k in range(parts)]
    )
    shifted = shifted.reshape(parts * block, parts * chans)
    result = jnp.dot(filt, shifted, preferred_element_type=jnp.float32)
    result = result.astype(jnp.bfloat16).T.reshape(parts, chans, block)
    back = lax.all_to_all(result, "seq", 0, 0, tiled=True)
    return back.reshape(parts * chans, block).T


def on_device(query_in, key_in, value_in, short_weight, long_filter, skip_gain, w_out):
    local_len, width = query_in.shape
    stacked = jnp.stack([query_in, key_in, value_in])
    border = passed_along(stacked[:, local_len - (KW - 1) :, :], "seq", 1)
    extended = jnp.concatenate([border, stacked], axis=1)
    convolved = short_weight[:, 0, None, :] * extended[:, KW - 1 : KW - 1 + local_len, :].astype(
        jnp.float32
    )
    for shift in range(1, KW):
        convolved = convolved + short_weight[:, shift, None, :] * extended[
            :, KW - 1 - shift : KW - 1 - shift + local_len, :
        ].astype(jnp.float32)
    query_conv = convolved[0].astype(jnp.bfloat16)
    gated = (convolved[1] * convolved[2]).astype(jnp.bfloat16)
    conv = long_conv(gated, long_filter)
    mixed = (
        query_conv.astype(jnp.float32)
        * (conv.astype(jnp.float32) + skip_gain * gated.astype(jnp.float32))
    ).astype(jnp.bfloat16)
    gathered = lax.all_gather(w_out, "seq", axis=1, tiled=True)
    halves = lax.axis_size("xh")
    quarters = lax.axis_size("y")
    gathered = gathered.reshape(width, halves, quarters, -1)
    terms = jnp.einsum("pc,cxyn->pyxn", mixed, gathered, preferred_element_type=jnp.float32)
    terms = terms.astype(jnp.bfloat16).reshape(local_len, -1)
    terms = lax.psum_scatter(terms, "y", scatter_dimension=1, tiled=True)
    return lax.psum_scatter(terms, "xh", scatter_dimension=1, tiled=True)


def solution(mesh):
    seq_size, chan_size = mesh.devices.shape
    split = Mesh(mesh.devices.reshape(seq_size, 2, chan_size // 2), ("seq", "xh", "y"))
    chan = ("xh", "y")
    placed = (
        P("seq", chan),
        P("seq", chan),
        P("seq", chan),
        P(None, None, chan),
        P(chan, "seq"),
        P(chan),
        P(chan, "seq"),
    )
    return jax.shard_map(
        on_device, mesh=split, in_specs=placed, out_specs=P("seq", chan), check_vma=False
    )
```

```python
import jax
import jax.numpy as jnp
from jax import lax
from jax.sharding import PartitionSpec as P

GROUP = 16
KW = 3


def passed_along(value, axis, by):
    devices = lax.axis_size(axis)
    pairs = [(i, i + by) for i in range(devices) if 0 <= i + by < devices]
    return lax.ppermute(value, axis, pairs)


def toeplitz_blocks(h, parts, block):
    flipped = jnp.concatenate([h[::-1], jnp.zeros((block,), h.dtype)])
    pieces = flipped.reshape(parts + 1, block)[::-1]
    windows = jnp.concatenate([pieces[1:], pieces[:-1]], axis=1)[:, : 2 * block - 1]
    rows = windows.astype(jnp.bfloat16)[None]
    step = 1
    while rows.shape[0] < block:
        width = rows.shape[2] - step
        rows = jnp.concatenate([rows[:, :, step : step + width], rows[:, :, :width]], axis=0)
        step *= 2
    return rows.reshape(block, parts * block)


def long_conv(gated, long_filter):
    block, width = gated.shape
    parts = lax.axis_size("seq")
    sent = gated.T.reshape(parts, width // parts, block)
    signal = lax.all_to_all(sent, "seq", 0, 0, tiled=True)
    taps = lax.all_to_all(long_filter, "seq", 0, 1, tiled=True)
    chans = signal.shape[1]
    filt = toeplitz_blocks(taps[0], parts, block)
    rows = jnp.transpose(signal, (2, 0, 1)).reshape(block, parts * chans)
    padded = jnp.concatenate([jnp.zeros((block, (parts - 1) * chans), rows.dtype), rows], axis=1)
    shifted = jnp.stack(
        [padded[:, (parts - 1 - k) * chans : (2 * parts - 1 - k) * chans] for k in range(parts)]
    )
    shifted = shifted.reshape(parts * block, parts * chans)
    result = jnp.dot(filt, shifted, preferred_element_type=jnp.float32)
    result = result.astype(jnp.bfloat16).T.reshape(parts, chans, block)
    back = lax.all_to_all(result, "seq", 0, 0, tiled=True)
    return back.reshape(parts * chans, block).T


def on_device(query_in, key_in, value_in, short_weight, long_filter, skip_gain, w_out):
    local_len, width = query_in.shape
    stacked = jnp.stack([query_in, key_in, value_in])
    border = passed_along(stacked[:, local_len - (KW - 1) :, :], "seq", 1)
    extended = jnp.concatenate([border, stacked], axis=1)
    convolved = short_weight[:, 0, None, :] * extended[:, KW - 1 : KW - 1 + local_len, :].astype(
        jnp.float32
    )
    for shift in range(1, KW):
        convolved = convolved + short_weight[:, shift, None, :] * extended[
            :, KW - 1 - shift : KW - 1 - shift + local_len, :
        ].astype(jnp.float32)
    query_conv = convolved[0].astype(jnp.bfloat16)
    gated = (convolved[1] * convolved[2]).astype(jnp.bfloat16)
    conv = long_conv(gated, long_filter)
    mixed = (
        query_conv.astype(jnp.float32)
        * (conv.astype(jnp.float32) + skip_gain * gated.astype(jnp.float32))
    ).astype(jnp.bfloat16)
    gathered = lax.all_gather(w_out, "seq", axis=1, tiled=True)
    split = local_len // 2
    first = jnp.dot(mixed[:split], gathered, preferred_element_type=jnp.float32)
    first = lax.psum_scatter(first.astype(jnp.bfloat16), "chan", scatter_dimension=1, tiled=True)
    second = jnp.dot(mixed[split:], gathered, preferred_element_type=jnp.float32)
    members = lax.axis_size("chan")
    second = second.astype(jnp.bfloat16).reshape(local_len - split, members, -1)
    second = lax.all_to_all(second, "chan", 1, 1)
    second = jnp.sum(second.astype(jnp.float32), axis=1).astype(jnp.bfloat16)
    return jnp.concatenate([first, second], axis=0)


def solution(mesh):
    placed = (
        P("seq", "chan"),
        P("seq", "chan"),
        P("seq", "chan"),
        P(None, None, "chan"),
        P("chan", "seq"),
        P("chan"),
        P("chan", "seq"),
    )
    return jax.shard_map(
        on_device, mesh=mesh, in_specs=placed, out_specs=P("seq", "chan"), check_vma=False
    )
```

```python
import jax
import jax.numpy as jnp
from jax import lax
from jax.sharding import PartitionSpec as P

GROUP = 16
KW = 3


def passed_along(value, axis, by):
    devices = lax.axis_size(axis)
    pairs = [(i, i + by) for i in range(devices) if 0 <= i + by < devices]
    return lax.ppermute(value, axis, pairs)


def toeplitz_blocks(h, parts, block):
    flipped = jnp.concatenate([h[::-1], jnp.zeros((block,), h.dtype)])
    pieces = flipped.reshape(parts + 1, block)[::-1]
    windows = jnp.concatenate([pieces[1:], pieces[:-1]], axis=1)[:, : 2 * block - 1]
    rows = windows.astype(jnp.bfloat16)[None]
    step = 1
    while rows.shape[0] < block:
        width = rows.shape[2] - step
        rows = jnp.concatenate([rows[:, :, step : step + width], rows[:, :, :width]], axis=0)
        step *= 2
    return rows.reshape(block, parts * block)


def long_conv(gated, long_filter):
    block, width = gated.shape
    parts = lax.axis_size("seq")
    sent = gated.T.reshape(parts, width // parts, block)
    signal = lax.all_to_all(sent, "seq", 0, 0, tiled=True)
    taps = lax.all_to_all(long_filter, "seq", 0, 1, tiled=True)
    chans = signal.shape[1]
    filt = toeplitz_blocks(taps[0], parts, block)
    rows = jnp.transpose(signal, (2, 0, 1)).reshape(block, parts * chans)
    padded = jnp.concatenate([jnp.zeros((block, (parts - 1) * chans), rows.dtype), rows], axis=1)
    shifted = jnp.stack(
        [padded[:, (parts - 1 - k) * chans : (2 * parts - 1 - k) * chans] for k in range(parts)]
    )
    shifted = shifted.reshape(parts * block, parts * chans)
    result = jnp.dot(filt, shifted, preferred_element_type=jnp.float32)
    result = result.astype(jnp.bfloat16).T.reshape(parts, chans, block)
    back = lax.all_to_all(result, "seq", 0, 0, tiled=True)
    return back.reshape(parts * chans, block).T


def on_device(query_in, key_in, value_in, short_weight, long_filter, skip_gain, w_out):
    local_len, width = query_in.shape
    stacked = jnp.stack([query_in, key_in, value_in])
    border = passed_along(stacked[:, local_len - (KW - 1) :, :], "seq", 1)
    extended = jnp.concatenate([border, stacked], axis=1)
    convolved = short_weight[:, 0, None, :] * extended[:, KW - 1 : KW - 1 + local_len, :].astype(
        jnp.float32
    )
    for shift in range(1, KW):
        convolved = convolved + short_weight[:, shift, None, :] * extended[
            :, KW - 1 - shift : KW - 1 - shift + local_len, :
        ].astype(jnp.float32)
    query_conv = convolved[0].astype(jnp.bfloat16)
    gated = (convolved[1] * convolved[2]).astype(jnp.bfloat16)
    conv = long_conv(gated, long_filter)
    mixed = (
        query_conv.astype(jnp.float32)
        * (conv.astype(jnp.float32) + skip_gain * gated.astype(jnp.float32))
    ).astype(jnp.bfloat16)
    gathered = lax.all_gather(w_out, "seq", axis=1, tiled=True)
    terms = jnp.dot(mixed, gathered, preferred_element_type=jnp.float32)
    members = lax.axis_size("chan")
    terms = terms.astype(jnp.bfloat16).reshape(local_len, members, -1)
    terms = lax.all_to_all(terms, "chan", 1, 1)
    return jnp.sum(terms.astype(jnp.float32), axis=1).astype(jnp.bfloat16)


def solution(mesh):
    placed = (
        P("seq", "chan"),
        P("seq", "chan"),
        P("seq", "chan"),
        P(None, None, "chan"),
        P("chan", "seq"),
        P("chan"),
        P("chan", "seq"),
    )
    return jax.shard_map(
        on_device, mesh=mesh, in_specs=placed, out_specs=P("seq", "chan"), check_vma=False
    )
```

```python
import jax
import jax.numpy as jnp
from jax import lax
from jax.sharding import Mesh, PartitionSpec as P

GROUP = 16
KW = 3


def passed_along(value, axis, by):
    devices = lax.axis_size(axis)
    pairs = [(i, i + by) for i in range(devices) if 0 <= i + by < devices]
    return lax.ppermute(value, axis, pairs)


def toeplitz_blocks(h, parts, block):
    flipped = jnp.concatenate([h[::-1], jnp.zeros((block,), h.dtype)])
    pieces = flipped.reshape(parts + 1, block)[::-1]
    windows = jnp.concatenate([pieces[1:], pieces[:-1]], axis=1)[:, : 2 * block - 1]
    rows = windows.astype(jnp.bfloat16)[None]
    step = 1
    while rows.shape[0] < block:
        width = rows.shape[2] - step
        rows = jnp.concatenate([rows[:, :, step : step + width], rows[:, :, :width]], axis=0)
        step *= 2
    return rows.reshape(block, parts * block)


def long_conv(gated, long_filter):
    block, width = gated.shape
    parts = lax.axis_size("seq")
    sent = gated.T.reshape(parts, width // parts, block)
    signal = lax.all_to_all(sent, "seq", 0, 0, tiled=True)
    taps = lax.all_to_all(long_filter, "seq", 0, 1, tiled=True)
    chans = signal.shape[1]
    filt = toeplitz_blocks(taps[0], parts, block)
    rows = jnp.transpose(signal, (2, 0, 1)).reshape(block, parts * chans)
    padded = jnp.concatenate([jnp.zeros((block, (parts - 1) * chans), rows.dtype), rows], axis=1)
    shifted = jnp.stack(
        [padded[:, (parts - 1 - k) * chans : (2 * parts - 1 - k) * chans] for k in range(parts)]
    )
    shifted = shifted.reshape(parts * block, parts * chans)
    result = jnp.dot(filt, shifted, preferred_element_type=jnp.float32)
    result = result.astype(jnp.bfloat16).T.reshape(parts, chans, block)
    back = lax.all_to_all(result, "seq", 0, 0, tiled=True)
    return back.reshape(parts * chans, block).T


def on_device(query_in, key_in, value_in, short_weight, long_filter, skip_gain, w_out):
    local_len, width = query_in.shape
    stacked = jnp.stack([query_in, key_in, value_in])
    border = passed_along(stacked[:, local_len - (KW - 1) :, :], "seq", 1)
    extended = jnp.concatenate([border, stacked], axis=1)
    convolved = short_weight[:, 0, None, :] * extended[:, KW - 1 : KW - 1 + local_len, :].astype(
        jnp.float32
    )
    for shift in range(1, KW):
        convolved = convolved + short_weight[:, shift, None, :] * extended[
            :, KW - 1 - shift : KW - 1 - shift + local_len, :
        ].astype(jnp.float32)
    query_conv = convolved[0].astype(jnp.bfloat16)
    gated = (convolved[1] * convolved[2]).astype(jnp.bfloat16)
    conv = long_conv(gated, long_filter)
    mixed = (
        query_conv.astype(jnp.float32)
        * (conv.astype(jnp.float32) + skip_gain * gated.astype(jnp.float32))
    ).astype(jnp.bfloat16)
    return project(mixed, w_out)


def project(mixed, w_out):
    local_len, width = mixed.shape
    rows, cols = w_out.shape
    halves = lax.axis_size("xh")
    quarters = lax.axis_size("y")
    per_block = lax.axis_size("seq") // (halves * quarters)
    chunks = 2
    piece = cols // chunks
    mixed_y = lax.all_gather(mixed, "y", axis=1, tiled=True).reshape(local_len, quarters, width)
    outs = []
    for q in range(chunks):
        part = lax.all_gather(w_out[:, q * piece : (q + 1) * piece], "seq", axis=0)
        part = part.reshape(halves, quarters, per_block, rows, piece)
        part = lax.all_to_all(part, "y", 1, 1, tiled=True)
        outs.append(
            jnp.einsum("pyr,xyurt->pxut", mixed_y, part, preferred_element_type=jnp.float32)
        )
    partial = jnp.stack(outs, axis=3).astype(jnp.bfloat16).reshape(local_len, -1)
    return lax.psum_scatter(partial, "xh", scatter_dimension=1, tiled=True)


def solution(mesh):
    seq_size, chan_size = mesh.devices.shape
    split = Mesh(mesh.devices.reshape(seq_size, 2, chan_size // 2), ("seq", "xh", "y"))
    chan = ("xh", "y")
    placed = (
        P("seq", chan),
        P("seq", chan),
        P("seq", chan),
        P(None, None, chan),
        P(chan, "seq"),
        P(chan),
        P(chan, "seq"),
    )
    return jax.shard_map(
        on_device, mesh=split, in_specs=placed, out_specs=P("seq", chan), check_vma=False
    )
```

```python
import jax
import jax.numpy as jnp
from jax import lax
from jax.sharding import PartitionSpec as P

GROUP = 16
KW = 3


def passed_along(value, axis, by):
    devices = lax.axis_size(axis)
    pairs = [(i, i + by) for i in range(devices) if 0 <= i + by < devices]
    return lax.ppermute(value, axis, pairs)


def toeplitz_blocks(h, parts, block):
    flipped = jnp.concatenate([h[::-1], jnp.zeros((block,), h.dtype)])
    pieces = flipped.reshape(parts + 1, block)[::-1]
    windows = jnp.concatenate([pieces[1:], pieces[:-1]], axis=1)[:, : 2 * block - 1]
    rows = windows.astype(jnp.bfloat16)[None]
    step = 1
    while rows.shape[0] < block:
        width = rows.shape[2] - step
        rows = jnp.concatenate([rows[:, :, step : step + width], rows[:, :, :width]], axis=0)
        step *= 2
    return rows.reshape(block, parts * block)


def long_conv(gated, long_filter):
    block, width = gated.shape
    parts = lax.axis_size("seq")
    sent = gated.T.reshape(parts, width // parts, block)
    signal = lax.all_to_all(sent, "seq", 0, 0, tiled=True)
    taps = lax.all_to_all(long_filter, "seq", 0, 1, tiled=True)
    chans = signal.shape[1]
    filt = toeplitz_blocks(taps[0], parts, block)
    rows = jnp.transpose(signal, (2, 0, 1)).reshape(block, parts * chans)
    padded = jnp.concatenate([jnp.zeros((block, (parts - 1) * chans), rows.dtype), rows], axis=1)
    shifted = jnp.stack(
        [padded[:, (parts - 1 - k) * chans : (2 * parts - 1 - k) * chans] for k in range(parts)]
    )
    shifted = shifted.reshape(parts * block, parts * chans)
    result = jnp.dot(filt, shifted, preferred_element_type=jnp.float32)
    result = result.astype(jnp.bfloat16).T.reshape(parts, chans, block)
    back = lax.all_to_all(result, "seq", 0, 0, tiled=True)
    return back.reshape(parts * chans, block).T


def on_device(query_in, key_in, value_in, short_weight, long_filter, skip_gain, w_out):
    local_len, width = query_in.shape
    stacked = jnp.stack([query_in, key_in, value_in])
    border = passed_along(stacked[:, local_len - (KW - 1) :, :], "seq", 1)
    extended = jnp.concatenate([border, stacked], axis=1)
    convolved = short_weight[:, 0, None, :] * extended[:, KW - 1 : KW - 1 + local_len, :].astype(
        jnp.float32
    )
    for shift in range(1, KW):
        convolved = convolved + short_weight[:, shift, None, :] * extended[
            :, KW - 1 - shift : KW - 1 - shift + local_len, :
        ].astype(jnp.float32)
    query_conv = convolved[0].astype(jnp.bfloat16)
    gated = (convolved[1] * convolved[2]).astype(jnp.bfloat16)
    conv = long_conv(gated, long_filter)
    mixed = (
        query_conv.astype(jnp.float32)
        * (conv.astype(jnp.float32) + skip_gain * gated.astype(jnp.float32))
    ).astype(jnp.bfloat16)
    gathered = lax.all_gather(w_out, "seq", axis=1, tiled=True)
    members = lax.axis_size("chan")
    gathered = gathered.reshape(width, members, -1)
    terms = jnp.einsum("pc,cbn->bpn", mixed, gathered, preferred_element_type=jnp.float32)
    terms = lax.all_to_all(terms.astype(jnp.bfloat16), "chan", 0, 0, tiled=True)
    return jnp.sum(terms.astype(jnp.float32), axis=0).astype(jnp.bfloat16)


def solution(mesh):
    placed = (
        P("seq", "chan"),
        P("seq", "chan"),
        P("seq", "chan"),
        P(None, None, "chan"),
        P("chan", "seq"),
        P("chan"),
        P("chan", "seq"),
    )
    return jax.shard_map(
        on_device, mesh=mesh, in_specs=placed, out_specs=P("seq", "chan"), check_vma=False
    )
```

```python
import jax
import jax.numpy as jnp
from jax import lax
from jax.sharding import PartitionSpec as P

GROUP = 16
KW = 3


def passed_along(value, axis, by):
    devices = lax.axis_size(axis)
    pairs = [(i, i + by) for i in range(devices) if 0 <= i + by < devices]
    return lax.ppermute(value, axis, pairs)


def toeplitz_blocks(h, parts, block):
    flipped = jnp.concatenate([h[::-1], jnp.zeros((block,), h.dtype)])
    pieces = flipped.reshape(parts + 1, block)[::-1]
    windows = jnp.concatenate([pieces[1:], pieces[:-1]], axis=1)[:, : 2 * block - 1]
    rows = windows.astype(jnp.bfloat16)[None]
    step = 1
    while rows.shape[0] < block:
        width = rows.shape[2] - step
        rows = jnp.concatenate([rows[:, :, step : step + width], rows[:, :, :width]], axis=0)
        step *= 2
    return rows.reshape(block, parts * block)


def conv_inputs(gated, long_filter):
    block, width = gated.shape
    parts = lax.axis_size("seq")
    sent = gated.T.reshape(parts, width // parts, block)
    signal = lax.all_to_all(sent, "seq", 0, 0, tiled=True)
    taps = lax.all_to_all(long_filter, "seq", 0, 1, tiled=True)
    chans = signal.shape[1]
    filt = toeplitz_blocks(taps[0], parts, block)
    rows = jnp.transpose(signal, (2, 0, 1)).reshape(block, parts * chans)
    padded = jnp.concatenate([jnp.zeros((block, (parts - 1) * chans), rows.dtype), rows], axis=1)
    shifted = jnp.stack(
        [padded[:, (parts - 1 - k) * chans : (2 * parts - 1 - k) * chans] for k in range(parts)]
    )
    return filt, shifted.reshape(parts * block, parts * chans)


def conv_rows(filt, shifted, parts):
    count = filt.shape[0]
    result = jnp.dot(filt, shifted, preferred_element_type=jnp.float32)
    result = result.astype(jnp.bfloat16).T.reshape(parts, -1, count)
    back = lax.all_to_all(result, "seq", 0, 0, tiled=True)
    return back.reshape(-1, count).T


def on_device(query_in, key_in, value_in, short_weight, long_filter, skip_gain, w_out):
    local_len, width = query_in.shape
    stacked = jnp.stack([query_in, key_in, value_in])
    border = passed_along(stacked[:, local_len - (KW - 1) :, :], "seq", 1)
    extended = jnp.concatenate([border, stacked], axis=1)
    convolved = short_weight[:, 0, None, :] * extended[:, KW - 1 : KW - 1 + local_len, :].astype(
        jnp.float32
    )
    for shift in range(1, KW):
        convolved = convolved + short_weight[:, shift, None, :] * extended[
            :, KW - 1 - shift : KW - 1 - shift + local_len, :
        ].astype(jnp.float32)
    query_conv = convolved[0].astype(jnp.bfloat16)
    gated = (convolved[1] * convolved[2]).astype(jnp.bfloat16)
    filt, shifted = conv_inputs(gated, long_filter)
    parts = lax.axis_size("seq")
    gathered = lax.all_gather(w_out, "seq", axis=1, tiled=True)
    members = lax.axis_size("chan")
    gathered = gathered.reshape(width, members, -1)
    halves = 2
    size = local_len // halves
    outs = []
    for h in range(halves):
        rows = slice(h * size, (h + 1) * size)
        conv = conv_rows(filt[rows], shifted, parts)
        mixed = (
            query_conv[rows].astype(jnp.float32)
            * (conv.astype(jnp.float32) + skip_gain * gated[rows].astype(jnp.float32))
        ).astype(jnp.bfloat16)
        terms = jnp.einsum("pc,cbn->bpn", mixed, gathered, preferred_element_type=jnp.float32)
        terms = lax.all_to_all(terms.astype(jnp.bfloat16), "chan", 0, 0, tiled=True)
        outs.append(jnp.sum(terms.astype(jnp.float32), axis=0).astype(jnp.bfloat16))
    return jnp.concatenate(outs, axis=0)


def solution(mesh):
    placed = (
        P("seq", "chan"),
        P("seq", "chan"),
        P("seq", "chan"),
        P(None, None, "chan"),
        P("chan", "seq"),
        P("chan"),
        P("chan", "seq"),
    )
    return jax.shard_map(
        on_device, mesh=mesh, in_specs=placed, out_specs=P("seq", "chan"), check_vma=False
    )
```

```python
import jax
import jax.numpy as jnp
from jax import lax
from jax.experimental import pallas as pl
from jax.experimental.pallas import tpu as pltpu
from jax.sharding import PartitionSpec as P

GROUP = 16
KW = 3


def passed_along(value, axis, by):
    devices = lax.axis_size(axis)
    pairs = [(i, i + by) for i in range(devices) if 0 <= i + by < devices]
    return lax.ppermute(value, axis, pairs)


def toeplitz_kernel(window_ref, signal_ref, out_ref):
    parts, span = window_ref.shape
    rows, block = signal_ref.shape
    chans = rows // parts
    out_ref[...] = jnp.zeros(out_ref.shape, out_ref.dtype)
    for k in range(parts):
        wide = jnp.broadcast_to(window_ref[k : k + 1, :], (block, span))
        taps = pltpu.roll(wide, span - block + 1, 1, stride=1, stride_axis=0)[:, :block]
        first = k * chans
        out_ref[first:, :] += jnp.dot(
            signal_ref[: rows - first, :],
            taps.astype(jnp.bfloat16),
            preferred_element_type=jnp.float32,
        )


def long_conv(gated, long_filter):
    block, width = gated.shape
    parts = lax.axis_size("seq")
    sent = gated.T.reshape(parts, width // parts, block)
    signal = lax.all_to_all(sent, "seq", 0, 0, tiled=True)
    taps = lax.all_to_all(long_filter, "seq", 0, 1, tiled=True)[0]
    chans = signal.shape[1]
    padded = jnp.concatenate(
        [jnp.zeros((block - 1,), taps.dtype), taps, jnp.zeros((1,), taps.dtype)]
    ).reshape(parts + 1, block)
    windows = jnp.concatenate([padded[:-1], padded[1:]], axis=1)
    rows = parts * chans
    result = pl.pallas_call(
        toeplitz_kernel,
        out_shape=jax.ShapeDtypeStruct((rows, block), jnp.float32),
        cost_estimate=pl.CostEstimate(
            flops=block * block * chans * parts * (parts + 1),
            transcendentals=0,
            bytes_accessed=windows.size * 4 + rows * block * 6,
        ),
    )(windows, signal.reshape(rows, block))
    result = result.astype(jnp.bfloat16).reshape(parts, chans, block)
    back = lax.all_to_all(result, "seq", 0, 0, tiled=True)
    return back.reshape(rows, block).T


def on_device(query_in, key_in, value_in, short_weight, long_filter, skip_gain, w_out):
    local_len, width = query_in.shape
    stacked = jnp.stack([query_in, key_in, value_in])
    border = passed_along(stacked[:, local_len - (KW - 1) :, :], "seq", 1)
    extended = jnp.concatenate([border, stacked], axis=1)
    convolved = short_weight[:, 0, None, :] * extended[:, KW - 1 : KW - 1 + local_len, :].astype(
        jnp.float32
    )
    for shift in range(1, KW):
        convolved = convolved + short_weight[:, shift, None, :] * extended[
            :, KW - 1 - shift : KW - 1 - shift + local_len, :
        ].astype(jnp.float32)
    query_conv = convolved[0].astype(jnp.bfloat16)
    gated = (convolved[1] * convolved[2]).astype(jnp.bfloat16)
    conv = long_conv(gated, long_filter)
    mixed = (
        query_conv.astype(jnp.float32)
        * (conv.astype(jnp.float32) + skip_gain * gated.astype(jnp.float32))
    ).astype(jnp.bfloat16)
    gathered = lax.all_gather(w_out, "seq", axis=1, tiled=True)
    members = lax.axis_size("chan")
    gathered = gathered.reshape(width, members, -1)
    terms = jnp.einsum("pc,cbn->bpn", mixed, gathered, preferred_element_type=jnp.float32)
    terms = lax.all_to_all(terms.astype(jnp.bfloat16), "chan", 0, 0, tiled=True)
    return jnp.sum(terms.astype(jnp.float32), axis=0).astype(jnp.bfloat16)


def solution(mesh):
    placed = (
        P("seq", "chan"),
        P("seq", "chan"),
        P("seq", "chan"),
        P(None, None, "chan"),
        P("chan", "seq"),
        P("chan"),
        P("chan", "seq"),
    )
    return jax.shard_map(
        on_device, mesh=mesh, in_specs=placed, out_specs=P("seq", "chan"), check_vma=False
    )
```

```python
import jax
import jax.numpy as jnp
from jax import lax
from jax.experimental import pallas as pl
from jax.experimental.pallas import tpu as pltpu
from jax.sharding import PartitionSpec as P

GROUP = 16
KW = 3


def passed_along(value, axis, by):
    devices = lax.axis_size(axis)
    pairs = [(i, i + by) for i in range(devices) if 0 <= i + by < devices]
    return lax.ppermute(value, axis, pairs)


def toeplitz_kernel(window_ref, signal_ref, out_ref):
    parts, span = window_ref.shape
    rows, block = signal_ref.shape
    chans = rows // parts
    out_ref[...] = jnp.zeros(out_ref.shape, out_ref.dtype)
    for k in range(parts):
        wide = jnp.broadcast_to(window_ref[k : k + 1, :], (block, span))
        taps = pltpu.roll(wide, span - block + 1, 1, stride=1, stride_axis=0)[:, :block]
        first = k * chans
        out_ref[first:, :] += jnp.dot(
            signal_ref[: rows - first, :],
            taps.astype(jnp.bfloat16),
            preferred_element_type=jnp.float32,
        )


def long_conv(gated, long_filter):
    block, width = gated.shape
    parts = lax.axis_size("seq")
    sent = gated.T.reshape(parts, width // parts, block)
    signal = lax.all_to_all(sent, "seq", 0, 0, tiled=True)
    taps = lax.all_to_all(long_filter, "seq", 0, 1, tiled=True)[0]
    chans = signal.shape[1]
    padded = jnp.concatenate(
        [jnp.zeros((block - 1,), taps.dtype), taps, jnp.zeros((1,), taps.dtype)]
    ).reshape(parts + 1, block)
    windows = jnp.concatenate([padded[:-1], padded[1:]], axis=1)
    rows = parts * chans
    result = pl.pallas_call(
        toeplitz_kernel,
        out_shape=jax.ShapeDtypeStruct((rows, block), jnp.float32),
        cost_estimate=pl.CostEstimate(
            flops=block * block * chans * parts * (parts + 1),
            transcendentals=0,
            bytes_accessed=windows.size * 4 + rows * block * 6,
        ),
    )(windows, signal.reshape(rows, block))
    result = result.astype(jnp.bfloat16).reshape(parts, chans, block)
    back = lax.all_to_all(result, "seq", 0, 0, tiled=True)
    return back.reshape(rows, block).T


def on_device(query_in, key_in, value_in, short_weight, long_filter, skip_gain, w_out):
    local_len, width = query_in.shape
    stacked = jnp.stack([query_in, key_in, value_in])
    border = passed_along(stacked[:, local_len - (KW - 1) :, :], "seq", 1)
    extended = jnp.concatenate([border, stacked], axis=1)
    convolved = short_weight[:, 0, None, :] * extended[:, KW - 1 : KW - 1 + local_len, :].astype(
        jnp.float32
    )
    for shift in range(1, KW):
        convolved = convolved + short_weight[:, shift, None, :] * extended[
            :, KW - 1 - shift : KW - 1 - shift + local_len, :
        ].astype(jnp.float32)
    query_conv = convolved[0].astype(jnp.bfloat16)
    gated = (convolved[1] * convolved[2]).astype(jnp.bfloat16)
    conv = long_conv(gated, long_filter)
    mixed = (
        query_conv.astype(jnp.float32)
        * (conv.astype(jnp.float32) + skip_gain * gated.astype(jnp.float32))
    ).astype(jnp.bfloat16)
    gathered = lax.all_gather(w_out, "seq", axis=1, tiled=True)
    members = lax.axis_size("chan")
    gathered = gathered.reshape(width, members, -1)
    halves = 2
    size = local_len // halves
    outs = []
    for h in range(halves):
        terms = jnp.einsum(
            "pc,cbn->bpn", mixed[h * size : (h + 1) * size], gathered,
            preferred_element_type=jnp.float32,
        )
        terms = lax.all_to_all(terms.astype(jnp.bfloat16), "chan", 0, 0, tiled=True)
        outs.append(jnp.sum(terms.astype(jnp.float32), axis=0).astype(jnp.bfloat16))
    return jnp.concatenate(outs, axis=0)


def solution(mesh):
    placed = (
        P("seq", "chan"),
        P("seq", "chan"),
        P("seq", "chan"),
        P(None, None, "chan"),
        P("chan", "seq"),
        P("chan"),
        P("chan", "seq"),
    )
    return jax.shard_map(
        on_device, mesh=mesh, in_specs=placed, out_specs=P("seq", "chan"), check_vma=False
    )
```

```python
import jax
import jax.numpy as jnp
from jax import lax
from jax.experimental import pallas as pl
from jax.experimental.pallas import tpu as pltpu
from jax.sharding import Mesh, PartitionSpec as P

GROUP = 16
KW = 3


SEQ = ("sq", "core")


def passed_along(value, axis, by):
    devices = lax.axis_size("sq") * lax.axis_size("core")
    pairs = [(i, i + by) for i in range(devices) if 0 <= i + by < devices]
    return lax.ppermute(value, axis, pairs)


def toeplitz_kernel(window_ref, signal_ref, out_ref):
    parts, span = window_ref.shape
    rows, block = signal_ref.shape
    chans = rows // parts
    out_ref[...] = jnp.zeros(out_ref.shape, out_ref.dtype)
    for k in range(parts):
        wide = jnp.broadcast_to(window_ref[k : k + 1, :], (block, span))
        taps = pltpu.roll(wide, span - block + 1, 1, stride=1, stride_axis=0)[:, :block]
        first = k * chans
        out_ref[first:, :] += jnp.dot(
            signal_ref[: rows - first, :],
            taps.astype(jnp.bfloat16),
            preferred_element_type=jnp.float32,
        )


def long_conv(gated, long_filter):
    block, width = gated.shape
    parts = lax.axis_size("sq") * lax.axis_size("core")
    sent = gated.T.reshape(parts, width // parts, block)
    signal = lax.all_to_all(sent, SEQ, 0, 0, tiled=True)
    taps = lax.all_to_all(long_filter, SEQ, 0, 1, tiled=True)[0]
    chans = signal.shape[1]
    padded = jnp.concatenate(
        [jnp.zeros((block - 1,), taps.dtype), taps, jnp.zeros((1,), taps.dtype)]
    ).reshape(parts + 1, block)
    windows = jnp.concatenate([padded[:-1], padded[1:]], axis=1)
    rows = parts * chans
    result = pl.pallas_call(
        toeplitz_kernel,
        out_shape=jax.ShapeDtypeStruct((rows, block), jnp.float32),
        cost_estimate=pl.CostEstimate(
            flops=block * block * chans * parts * (parts + 1),
            transcendentals=0,
            bytes_accessed=windows.size * 4 + rows * block * 6,
        ),
    )(windows, signal.reshape(rows, block))
    result = result.astype(jnp.bfloat16).reshape(parts, chans, block)
    back = lax.all_to_all(result, SEQ, 0, 0, tiled=True)
    return back.reshape(rows, block).T


def on_device(query_in, key_in, value_in, short_weight, long_filter, skip_gain, w_out):
    local_len, width = query_in.shape
    stacked = jnp.stack([query_in, key_in, value_in])
    border = passed_along(stacked[:, local_len - (KW - 1) :, :], SEQ, 1)
    extended = jnp.concatenate([border, stacked], axis=1)
    convolved = short_weight[:, 0, None, :] * extended[:, KW - 1 : KW - 1 + local_len, :].astype(
        jnp.float32
    )
    for shift in range(1, KW):
        convolved = convolved + short_weight[:, shift, None, :] * extended[
            :, KW - 1 - shift : KW - 1 - shift + local_len, :
        ].astype(jnp.float32)
    query_conv = convolved[0].astype(jnp.bfloat16)
    gated = (convolved[1] * convolved[2]).astype(jnp.bfloat16)
    conv = long_conv(gated, long_filter)
    mixed = (
        query_conv.astype(jnp.float32)
        * (conv.astype(jnp.float32) + skip_gain * gated.astype(jnp.float32))
    ).astype(jnp.bfloat16)
    members = lax.axis_size("chan")
    cores = lax.axis_size("core")
    rows, cols = w_out.shape
    gathered = lax.all_gather(w_out, "sq", axis=1, tiled=True)
    gathered = lax.all_gather(gathered, "core", axis=0)
    per_member = lax.axis_size("sq") // members
    gathered = gathered.reshape(cores, rows, members, per_member, cols)
    gathered = jnp.transpose(gathered, (1, 2, 3, 0, 4)).reshape(rows, members, -1)
    halves = 2
    size = local_len // halves
    outs = []
    for h in range(halves):
        terms = jnp.einsum(
            "pc,cbn->bpn", mixed[h * size : (h + 1) * size], gathered,
            preferred_element_type=jnp.float32,
        )
        terms = lax.all_to_all(terms.astype(jnp.bfloat16), "chan", 0, 0, tiled=True)
        outs.append(jnp.sum(terms.astype(jnp.float32), axis=0).astype(jnp.bfloat16))
    return jnp.concatenate(outs, axis=0)


def solution(mesh):
    seq_size, chan_size = mesh.devices.shape
    split = Mesh(mesh.devices.reshape(seq_size // 2, 2, chan_size), ("sq", "core", "chan"))
    placed = (
        P(SEQ, "chan"),
        P(SEQ, "chan"),
        P(SEQ, "chan"),
        P(None, None, "chan"),
        P("chan", SEQ),
        P("chan"),
        P("chan", SEQ),
    )
    return jax.shard_map(
        on_device, mesh=split, in_specs=placed, out_specs=P(SEQ, "chan"), check_vma=False
    )
```

```python
import jax
import jax.numpy as jnp
from jax import lax
from jax.experimental import pallas as pl
from jax.experimental.pallas import tpu as pltpu
from jax.sharding import PartitionSpec as P

GROUP = 16
KW = 3


def passed_along(value, axis, by):
    devices = lax.axis_size(axis)
    pairs = [(i, i + by) for i in range(devices) if 0 <= i + by < devices]
    return lax.ppermute(value, axis, pairs)


def toeplitz_kernel(window_ref, signal_ref, out_ref, acc_ref):
    parts, span = window_ref.shape
    rows, block = signal_ref.shape
    chans = rows // parts
    acc_ref[...] = jnp.zeros(acc_ref.shape, acc_ref.dtype)
    for k in range(parts):
        wide = jnp.broadcast_to(window_ref[k : k + 1, :], (block, span))
        taps = pltpu.roll(wide, span - block + 1, 1, stride=1, stride_axis=0)[:, :block]
        first = k * chans
        acc_ref[first:, :] += jnp.dot(
            signal_ref[: rows - first, :],
            taps.astype(jnp.bfloat16),
            preferred_element_type=jnp.float32,
        )
    out_ref[...] = acc_ref[...].astype(out_ref.dtype)


def long_conv(gated, long_filter):
    block, width = gated.shape
    parts = lax.axis_size("seq")
    sent = gated.T.reshape(parts, width // parts, block)
    signal = lax.all_to_all(sent, "seq", 0, 0, tiled=True)
    taps = lax.all_to_all(long_filter, "seq", 0, 1, tiled=True)[0]
    chans = signal.shape[1]
    padded = jnp.concatenate(
        [jnp.zeros((block - 1,), taps.dtype), taps, jnp.zeros((1,), taps.dtype)]
    ).reshape(parts + 1, block)
    windows = jnp.concatenate([padded[:-1], padded[1:]], axis=1)
    rows = parts * chans
    result = pl.pallas_call(
        toeplitz_kernel,
        out_shape=jax.ShapeDtypeStruct((rows, block), jnp.bfloat16),
        scratch_shapes=[pltpu.VMEM((rows, block), jnp.float32)],
        cost_estimate=pl.CostEstimate(
            flops=block * block * chans * parts * (parts + 1),
            transcendentals=0,
            bytes_accessed=windows.size * 4 + rows * block * 6,
        ),
    )(windows, signal.reshape(rows, block))
    result = result.reshape(parts, chans, block)
    back = lax.all_to_all(result, "seq", 0, 0, tiled=True)
    return back.reshape(rows, block).T


def on_device(query_in, key_in, value_in, short_weight, long_filter, skip_gain, w_out):
    local_len, width = query_in.shape
    stacked = jnp.stack([query_in, key_in, value_in])
    border = passed_along(stacked[:, local_len - (KW - 1) :, :], "seq", 1)
    extended = jnp.concatenate([border, stacked], axis=1)
    convolved = short_weight[:, 0, None, :] * extended[:, KW - 1 : KW - 1 + local_len, :].astype(
        jnp.float32
    )
    for shift in range(1, KW):
        convolved = convolved + short_weight[:, shift, None, :] * extended[
            :, KW - 1 - shift : KW - 1 - shift + local_len, :
        ].astype(jnp.float32)
    query_conv = convolved[0].astype(jnp.bfloat16)
    gated = (convolved[1] * convolved[2]).astype(jnp.bfloat16)
    conv = long_conv(gated, long_filter)
    mixed = (
        query_conv.astype(jnp.float32)
        * (conv.astype(jnp.float32) + skip_gain * gated.astype(jnp.float32))
    ).astype(jnp.bfloat16)
    gathered = lax.all_gather(w_out, "seq", axis=1, tiled=True)
    members = lax.axis_size("chan")
    gathered = gathered.reshape(width, members, -1)
    halves = 2
    size = local_len // halves
    outs = []
    for h in range(halves):
        terms = jnp.einsum(
            "pc,cbn->bpn", mixed[h * size : (h + 1) * size], gathered,
            preferred_element_type=jnp.float32,
        )
        terms = lax.all_to_all(terms.astype(jnp.bfloat16), "chan", 0, 0, tiled=True)
        outs.append(jnp.sum(terms.astype(jnp.float32), axis=0).astype(jnp.bfloat16))
    return jnp.concatenate(outs, axis=0)


def solution(mesh):
    placed = (
        P("seq", "chan"),
        P("seq", "chan"),
        P("seq", "chan"),
        P(None, None, "chan"),
        P("chan", "seq"),
        P("chan"),
        P("chan", "seq"),
    )
    return jax.shard_map(
        on_device, mesh=mesh, in_specs=placed, out_specs=P("seq", "chan"), check_vma=False
    )
```

```python
import jax
import jax.numpy as jnp
from jax import lax
from jax.experimental import pallas as pl
from jax.experimental.pallas import tpu as pltpu
from jax.sharding import PartitionSpec as P

GROUP = 16
KW = 3


def passed_along(value, axis, by):
    devices = lax.axis_size(axis)
    pairs = [(i, i + by) for i in range(devices) if 0 <= i + by < devices]
    return lax.ppermute(value, axis, pairs)


def toeplitz_kernel(window_ref, signal_ref, out_ref, acc_ref):
    parts, span = window_ref.shape
    rows, block = signal_ref.shape
    chans = rows // parts
    acc_ref[...] = jnp.zeros(acc_ref.shape, acc_ref.dtype)
    for k in range(parts):
        wide = jnp.broadcast_to(window_ref[k : k + 1, :], (block, span))
        taps = pltpu.roll(wide, span - block + 1, 1, stride=1, stride_axis=0)[:, :block]
        first = k * chans
        acc_ref[first:, :] += jnp.dot(
            signal_ref[: rows - first, :],
            taps.astype(jnp.bfloat16),
            preferred_element_type=jnp.float32,
        )
    out_ref[...] = acc_ref[...].astype(out_ref.dtype)


def long_conv(gated, long_filter):
    block, width = gated.shape
    parts = lax.axis_size("seq")
    sent = gated.T.reshape(parts, width // parts, block)
    signal = lax.all_to_all(sent, "seq", 0, 0, tiled=True)
    taps = lax.all_to_all(long_filter, "seq", 0, 1, tiled=True)[0]
    chans = signal.shape[1]
    padded = jnp.concatenate(
        [jnp.zeros((block - 1,), taps.dtype), taps, jnp.zeros((1,), taps.dtype)]
    ).reshape(parts + 1, block)
    windows = jnp.concatenate([padded[:-1], padded[1:]], axis=1)
    rows = parts * chans
    result = pl.pallas_call(
        toeplitz_kernel,
        out_shape=jax.ShapeDtypeStruct((rows, block), jnp.bfloat16),
        scratch_shapes=[pltpu.VMEM((rows, block), jnp.float32)],
        cost_estimate=pl.CostEstimate(
            flops=block * block * chans * parts * (parts + 1),
            transcendentals=0,
            bytes_accessed=windows.size * 4 + rows * block * 6,
        ),
    )(windows, signal.reshape(rows, block))
    result = result.reshape(parts, chans, block)
    back = lax.all_to_all(result, "seq", 0, 0, tiled=True)
    return back.reshape(rows, block).T


def on_device(query_in, key_in, value_in, short_weight, long_filter, skip_gain, w_out):
    local_len, width = query_in.shape
    stacked = jnp.stack([query_in, key_in, value_in])
    border = passed_along(stacked[:, local_len - (KW - 1) :, :], "seq", 1)
    extended = jnp.concatenate([border, stacked], axis=1)
    def short(which):
        total = short_weight[which, 0, None, :] * extended[
            which, KW - 1 : KW - 1 + local_len, :
        ].astype(jnp.float32)
        for shift in range(1, KW):
            total = total + short_weight[which, shift, None, :] * extended[
                which, KW - 1 - shift : KW - 1 - shift + local_len, :
            ].astype(jnp.float32)
        return total

    gated = (short(1) * short(2)).astype(jnp.bfloat16)
    conv = long_conv(gated, long_filter)
    query_conv = short(0).astype(jnp.bfloat16)
    mixed = (
        query_conv.astype(jnp.float32)
        * (conv.astype(jnp.float32) + skip_gain * gated.astype(jnp.float32))
    ).astype(jnp.bfloat16)
    gathered = lax.all_gather(w_out, "seq", axis=1, tiled=True)
    members = lax.axis_size("chan")
    gathered = gathered.reshape(width, members, -1)
    bounds = (0, local_len // 4, local_len)
    outs = []
    for h in range(len(bounds) - 1):
        terms = jnp.einsum(
            "pc,cbn->bpn", mixed[bounds[h] : bounds[h + 1]], gathered,
            preferred_element_type=jnp.float32,
        )
        terms = lax.all_to_all(terms.astype(jnp.bfloat16), "chan", 0, 0, tiled=True)
        outs.append(jnp.sum(terms.astype(jnp.float32), axis=0).astype(jnp.bfloat16))
    return jnp.concatenate(outs, axis=0)


def solution(mesh):
    placed = (
        P("seq", "chan"),
        P("seq", "chan"),
        P("seq", "chan"),
        P(None, None, "chan"),
        P("chan", "seq"),
        P("chan"),
        P("chan", "seq"),
    )
    return jax.shard_map(
        on_device, mesh=mesh, in_specs=placed, out_specs=P("seq", "chan"), check_vma=False
    )
```

```python
import jax
import jax.numpy as jnp
from jax import lax
from jax.experimental import pallas as pl
from jax.experimental.pallas import tpu as pltpu
from jax.sharding import PartitionSpec as P

GROUP = 16
KW = 3


def passed_along(value, axis, by):
    devices = lax.axis_size(axis)
    pairs = [(i, i + by) for i in range(devices) if 0 <= i + by < devices]
    return lax.ppermute(value, axis, pairs)


def toeplitz_kernel(window_ref, signal_ref, out_ref, acc_ref):
    parts, span = window_ref.shape
    rows, block = signal_ref.shape
    chans = rows // parts
    acc_ref[...] = jnp.zeros(acc_ref.shape, acc_ref.dtype)
    for k in range(parts):
        wide = jnp.broadcast_to(window_ref[k : k + 1, :], (block, span))
        taps = pltpu.roll(wide, span - block + 1, 1, stride=1, stride_axis=0)[:, :block]
        first = k * chans
        acc_ref[first:, :] += jnp.dot(
            signal_ref[: rows - first, :],
            taps.astype(jnp.bfloat16),
            preferred_element_type=jnp.float32,
        )
    out_ref[...] = acc_ref[...].astype(out_ref.dtype)


def long_conv(gated, long_filter):
    block, width = gated.shape
    parts = lax.axis_size("seq")
    sent = gated.T.reshape(parts, width // parts, block)
    signal = lax.all_to_all(sent, "seq", 0, 0, tiled=True)
    taps = lax.all_to_all(long_filter, "seq", 0, 1, tiled=True)[0]
    chans = signal.shape[1]
    padded = jnp.concatenate(
        [jnp.zeros((block - 1,), taps.dtype), taps, jnp.zeros((1,), taps.dtype)]
    ).reshape(parts + 1, block)
    windows = jnp.concatenate([padded[:-1], padded[1:]], axis=1)
    rows = parts * chans
    result = pl.pallas_call(
        toeplitz_kernel,
        out_shape=jax.ShapeDtypeStruct((rows, block), jnp.bfloat16),
        scratch_shapes=[pltpu.VMEM((rows, block), jnp.float32)],
        cost_estimate=pl.CostEstimate(
            flops=block * block * chans * parts * (parts + 1),
            transcendentals=0,
            bytes_accessed=windows.size * 4 + rows * block * 6,
        ),
    )(windows, signal.reshape(rows, block))
    result = result.reshape(parts, chans, block)
    back = lax.all_to_all(result, "seq", 0, 0, tiled=True)
    return lax.optimization_barrier(back.reshape(rows, block).T)


def on_device(query_in, key_in, value_in, short_weight, long_filter, skip_gain, w_out):
    local_len, width = query_in.shape
    stacked = jnp.stack([query_in, key_in, value_in])
    border = passed_along(stacked[:, local_len - (KW - 1) :, :], "seq", 1)
    extended = jnp.concatenate([border, stacked], axis=1)
    convolved = short_weight[:, 0, None, :] * extended[:, KW - 1 : KW - 1 + local_len, :].astype(
        jnp.float32
    )
    for shift in range(1, KW):
        convolved = convolved + short_weight[:, shift, None, :] * extended[
            :, KW - 1 - shift : KW - 1 - shift + local_len, :
        ].astype(jnp.float32)
    query_conv = convolved[0].astype(jnp.bfloat16)
    gated = (convolved[1] * convolved[2]).astype(jnp.bfloat16)
    conv = long_conv(gated, long_filter)
    mixed = (
        query_conv.astype(jnp.float32)
        * (conv.astype(jnp.float32) + skip_gain * gated.astype(jnp.float32))
    ).astype(jnp.bfloat16)
    gathered = lax.all_gather(w_out, "seq", axis=1, tiled=True)
    members = lax.axis_size("chan")
    gathered = gathered.reshape(width, members, -1)
    halves = 2
    size = local_len // halves
    outs = []
    for h in range(halves):
        terms = jnp.einsum(
            "pc,cbn->bpn", mixed[h * size : (h + 1) * size], gathered,
            preferred_element_type=jnp.float32,
        )
        terms = lax.all_to_all(terms.astype(jnp.bfloat16), "chan", 0, 0, tiled=True)
        outs.append(jnp.sum(terms.astype(jnp.float32), axis=0).astype(jnp.bfloat16))
    return jnp.concatenate(outs, axis=0)


def solution(mesh):
    placed = (
        P("seq", "chan"),
        P("seq", "chan"),
        P("seq", "chan"),
        P(None, None, "chan"),
        P("chan", "seq"),
        P("chan"),
        P("chan", "seq"),
    )
    return jax.shard_map(
        on_device, mesh=mesh, in_specs=placed, out_specs=P("seq", "chan"), check_vma=False
    )
```

```python
import jax
import jax.numpy as jnp
from jax import lax
from jax.experimental import pallas as pl
from jax.experimental.pallas import tpu as pltpu
from jax.sharding import PartitionSpec as P

GROUP = 16
KW = 3


def passed_along(value, axis, by):
    devices = lax.axis_size(axis)
    pairs = [(i, i + by) for i in range(devices) if 0 <= i + by < devices]
    return lax.ppermute(value, axis, pairs)


def toeplitz_kernel(window_ref, signal_ref, out_ref, acc_ref):
    parts, span = window_ref.shape
    rows, block = signal_ref.shape
    chans = rows // parts
    acc_ref[...] = jnp.zeros(acc_ref.shape, acc_ref.dtype)
    for k in range(parts):
        wide = jnp.broadcast_to(window_ref[k : k + 1, :], (block, span))
        taps = pltpu.roll(wide, span - block + 1, 1, stride=1, stride_axis=0)[:, :block]
        first = k * chans
        acc_ref[first:, :] += jnp.dot(
            signal_ref[: rows - first, :],
            taps.astype(jnp.bfloat16),
            preferred_element_type=jnp.float32,
        )
    out_ref[...] = acc_ref[...].astype(out_ref.dtype)


def long_conv(gated, long_filter):
    block, width = gated.shape
    parts = lax.axis_size("seq")
    sent = gated.T.reshape(parts, width // parts, block)
    signal = lax.all_to_all(sent, "seq", 0, 0, tiled=True)
    taps = lax.all_to_all(long_filter, "seq", 0, 1, tiled=True)[0]
    chans = signal.shape[1]
    padded = jnp.concatenate(
        [jnp.zeros((block - 1,), taps.dtype), taps, jnp.zeros((1,), taps.dtype)]
    ).reshape(parts + 1, block)
    windows = jnp.concatenate([padded[:-1], padded[1:]], axis=1)
    rows = parts * chans
    result = pl.pallas_call(
        toeplitz_kernel,
        out_shape=jax.ShapeDtypeStruct((rows, block), jnp.bfloat16),
        scratch_shapes=[pltpu.VMEM((rows, block), jnp.float32)],
        cost_estimate=pl.CostEstimate(
            flops=block * block * chans * parts * (parts + 1),
            transcendentals=0,
            bytes_accessed=windows.size * 4 + rows * block * 6,
        ),
    )(windows, signal.reshape(rows, block))
    result = result.reshape(parts, chans, block)
    back = lax.all_to_all(result, "seq", 0, 0, tiled=True)
    return lax.optimization_barrier(back.reshape(rows, block).T)


def on_device(query_in, key_in, value_in, short_weight, long_filter, skip_gain, w_out):
    local_len, width = query_in.shape
    stacked = jnp.stack([query_in, key_in, value_in])
    border = passed_along(stacked[:, local_len - (KW - 1) :, :], "seq", 1)
    extended = jnp.concatenate([border, stacked], axis=1)
    convolved = short_weight[:, 0, None, :] * extended[:, KW - 1 : KW - 1 + local_len, :].astype(
        jnp.float32
    )
    for shift in range(1, KW):
        convolved = convolved + short_weight[:, shift, None, :] * extended[
            :, KW - 1 - shift : KW - 1 - shift + local_len, :
        ].astype(jnp.float32)
    query_conv = convolved[0].astype(jnp.bfloat16)
    gated = (convolved[1] * convolved[2]).astype(jnp.bfloat16)
    conv = long_conv(gated, long_filter)
    mixed = (
        query_conv.astype(jnp.float32)
        * (conv.astype(jnp.float32) + skip_gain * gated.astype(jnp.float32))
    ).astype(jnp.bfloat16)
    gathered = lax.all_gather(w_out, "seq", axis=1, tiled=True)
    members = lax.axis_size("chan")
    gathered = gathered.reshape(width, members, -1)
    bounds = (0, local_len // 4, local_len)
    outs = []
    for h in range(len(bounds) - 1):
        terms = jnp.einsum(
            "pc,cbn->bpn", mixed[bounds[h] : bounds[h + 1]], gathered,
            preferred_element_type=jnp.float32,
        )
        terms = lax.all_to_all(terms.astype(jnp.bfloat16), "chan", 0, 0, tiled=True)
        outs.append(jnp.sum(terms.astype(jnp.float32), axis=0).astype(jnp.bfloat16))
    return jnp.concatenate(outs, axis=0)


def solution(mesh):
    placed = (
        P("seq", "chan"),
        P("seq", "chan"),
        P("seq", "chan"),
        P(None, None, "chan"),
        P("chan", "seq"),
        P("chan"),
        P("chan", "seq"),
    )
    return jax.shard_map(
        on_device, mesh=mesh, in_specs=placed, out_specs=P("seq", "chan"), check_vma=False
    )
```
